512 devices in a mesh: dp: 4 (over z_hi, core), wide: 16 (over y, x), narrow: 8 (over z_lo).
Axes of the slice: x: 4, y: 4, z: 16 (z_hi: 2, z_lo: 8; z = z_hi * 8 + z_lo), core: 2. Of those that a mesh axis runs over, the one named last changes fastest.
Arguments:
- patches: bfloat16 [1024, 4, 6144], P('wide', 'dp'), parts along dimension 1, may hold values from -6 to 6
- vit_gain: float32 [6144], replicated, may hold values from 0.1 to 1.9
- vit_qkv: bfloat16 [6144, 3, 32, 128], P('narrow', None, 'wide'), may hold values from -4 to 4
- vit_in: bfloat16 [6144, 12288], P('narrow', 'wide'), may hold values from -0.078125 to 0.078125
- vit_attn_out: bfloat16 [4096, 6144], P('wide', 'narrow'), may hold values from -1 to 1
- vit_mlp_out: bfloat16 [12288, 6144], P('wide', 'narrow'), may hold values from -0.109375 to 0.109375
- proj: bfloat16 [6144, 4096], P('narrow', 'wide'), may hold values from -0.01953125 to 0.01953125
Outputs:
- encoded: bfloat16 [1024, 4, 4096], P('wide', 'dp', 'narrow'), parts along dimension 1
The draws below stay inside these ranges and needn't reach their ends.
There are 4 independent parts, one for each index of `dp`. The reference program is written for one: setup_inputs(seed, part) draws one part's arguments, and reference() takes and returns one part's arrays. A program takes and returns all parts, laid end to end along the dimension named above; an argument that names none is the same for every part. Nothing has to cross between parts.
All inputs are finite; a program needn't handle non-finite values.
Results may differ from the reference program's by a relative error of at most 0.035.
Values may be sent and summed in bfloat16 or wider, within the bound.
No kernel may reach another device: no remote copies, remote signals or barrier semaphores. Data moves between devices by JAX's collectives and lax.ppermute only.
A program may use at most 64 MiB of HBM per device.

```python
import math
import jax
import jax.numpy as jnp
from jax import lax

D = 6144
FF = 12288
HV = 32
DH = 128
E = 4096
P_SIZE = 1024
IMG = 1
N_WIDE = 16
N_NARROW = 8


def draw_vit_qkv(key, part):
    base_key = jax.random.fold_in(key, 0)
    values = jnp.clip(jax.random.normal(base_key, (D, 3, HV, DH), jnp.float32), -6.0, 6.0) * D ** (-0.5)
    return values.astype(jnp.bfloat16)


def shard_levels(key, extent, cuts, low, largest):
    def one(position, shards_of):
        draws = jax.random.uniform(jax.random.fold_in(jax.random.fold_in(key, 6), position), (shards_of,), jnp.float32, low / len(cuts), largest / len(cuts))
        return jnp.repeat(jnp.exp(draws), extent[position] // shards_of).reshape((-1,) + (1,) * (len(extent) - position - 1))

    gain = one(*cuts[0])
    for cut in cuts[1:]:
        gain = gain * one(*cut)
    return gain


def gaussian(key, extent, scale, limit, pieces=(), kind=jnp.bfloat16):
    drawn = scale * jax.random.normal(key, extent, jnp.float32)
    if pieces:
        drawn = drawn * shard_levels(key, extent, pieces, -0.22, 0.18)
    return jnp.clip(drawn, -limit, limit).astype(kind)


def setup_inputs(seed: int = 0, part: int = 0) -> dict:
    seeds = jax.random.split(jax.random.key(seed), 8)
    own_keys = jax.random.split(jax.random.fold_in(seeds[7], part), 8)
    patches = gaussian(own_keys[0], (P_SIZE, IMG, D), 1.0, 6.0, ((0, 16),))
    vit_gain = jnp.clip(1.0 + 0.18 * jax.random.normal(seeds[1], (D,), jnp.float32), 0.1, 1.9)
    vit_qkv = draw_vit_qkv(jax.random.fold_in(seeds[7], 71), part)
    vit_in = gaussian(seeds[3], (D, FF), D ** -0.5, 0.078125, ((0, 8), (1, 16)))
    vit_attn_out = gaussian(seeds[4], (HV * DH, D), 0.0625, 1.0, ((0, 16), (1, 8)))
    vit_mlp_out = gaussian(seeds[5], (FF, D), (FF // 4) ** -0.5, 0.109375, ((0, 16), (1, 8)))
    proj = gaussian(seeds[6], (D, E), (16 * D) ** -0.5, 0.01953125, ((0, 8), (1, 16)))
    return dict(patches=patches, vit_gain=vit_gain, vit_qkv=vit_qkv, vit_in=vit_in, vit_attn_out=vit_attn_out, vit_mlp_out=vit_mlp_out, proj=proj)


def layer_norm(inputs, gain_row):
    widened = inputs.astype(jnp.float32)
    centred = widened - lax.optimization_barrier(jnp.mean(widened, axis=-1, keepdims=True))
    variance = lax.optimization_barrier(jnp.mean(centred * centred, axis=-1, keepdims=True))
    return (centred * lax.rsqrt(variance + 1e-06) * gain_row).astype(jnp.bfloat16)

def block_sum(pairs, blocks):
    row_count = pairs[0][0].shape[0]
    col_count = pairs[0][1].shape[1]

    def add_block(running, block_index):
        partial_sum = jnp.zeros((row_count, col_count), jnp.float32)
        for left_part, right_part in pairs:
            block_width = left_part.shape[1] // blocks
            first = (block_index * block_width).astype(jnp.int32)
            left_block = lax.dynamic_slice_in_dim(left_part, first, block_width, 1)
            right_block = lax.dynamic_slice_in_dim(right_part, first, block_width, 0)
            partial_sum = partial_sum + jnp.dot(left_block, right_block, preferred_element_type=jnp.float32)
        rounded = lax.optimization_barrier(partial_sum.astype(jnp.bfloat16))
        return (running + rounded.astype(jnp.float32), None)
    start_sum = jnp.zeros((row_count, col_count), jnp.float32)
    result, _ = lax.scan(add_block, start_sum, jnp.arange(blocks, dtype=jnp.int32))
    return result

def attend(queries, keys_all, values_all):
    score_scale = 1.0 / math.sqrt(queries.shape[-1])
    scores = jnp.einsum('pihd,qihd->ihpq', queries.astype(jnp.float32), keys_all.astype(jnp.float32)) * score_scale
    highest = lax.optimization_barrier(jnp.max(scores, axis=-1, keepdims=True))
    exponentials = jnp.exp(scores - highest)
    totals = lax.optimization_barrier(jnp.sum(exponentials, axis=-1))
    weights = lax.optimization_barrier(exponentials.astype(jnp.bfloat16))
    mixed_sum = jnp.einsum('ihpq,qihd->pihd', weights.astype(jnp.float32), values_all.astype(jnp.float32))
    return (mixed_sum / jnp.transpose(totals, (2, 0, 1))[..., None]).astype(jnp.bfloat16)

def reference(patches, vit_gain, vit_qkv, vit_in, vit_attn_out, vit_mlp_out, proj):
    normed = layer_norm(patches, vit_gain).reshape(P_SIZE * IMG, D)
    qkv_sum = block_sum(((normed, vit_qkv.reshape(D, 3 * HV * DH)),), N_NARROW)
    hidden_sum = block_sum(((normed, vit_in),), N_NARROW)
    qkv_all = lax.optimization_barrier(qkv_sum.astype(jnp.bfloat16)).reshape(P_SIZE, IMG, 3, HV, DH)
    activated = jax.nn.gelu(hidden_sum, approximate=False).astype(jnp.bfloat16)
    mixed = attend(qkv_all[:, :, 0], qkv_all[:, :, 1], qkv_all[:, :, 2]).reshape(P_SIZE * IMG, HV * DH)
    branch_sum = block_sum(((mixed, vit_attn_out), (activated, vit_mlp_out)), N_WIDE)
    vit_output = (patches.reshape(P_SIZE * IMG, D).astype(jnp.float32) + branch_sum).astype(jnp.bfloat16)
    encoded = block_sum(((vit_output, proj),), N_NARROW)
    return encoded.astype(jnp.bfloat16).reshape(P_SIZE, IMG, E)
```

```python
import math

import jax
import jax.numpy as jnp
from jax import lax
from jax.sharding import PartitionSpec as P


def layer_norm(inputs, gain_row):
    widened = inputs.astype(jnp.float32)
    centred = widened - jnp.mean(widened, axis=-1, keepdims=True)
    variance = jnp.mean(centred * centred, axis=-1, keepdims=True)
    return (centred * lax.rsqrt(variance + 1e-06) * gain_row).astype(jnp.bfloat16)


def attend(queries, keys_all, values_all):
    score_scale = 1.0 / math.sqrt(queries.shape[-1])
    scores = (
        jnp.einsum("pihd,qihd->ihpq", queries, keys_all, preferred_element_type=jnp.float32)
        * score_scale
    )
    highest = jnp.max(scores, axis=-1, keepdims=True)
    exponentials = jnp.exp(scores - highest)
    totals = jnp.sum(exponentials, axis=-1)
    weights = exponentials.astype(jnp.bfloat16)
    mixed_sum = jnp.einsum(
        "ihpq,qihd->pihd", weights, values_all, preferred_element_type=jnp.float32
    )
    return (mixed_sum / jnp.transpose(totals, (2, 0, 1))[..., None]).astype(jnp.bfloat16)


def gather_wide(block, n_wide):
    spread = jnp.broadcast_to(block[None], (n_wide,) + block.shape)
    got = lax.all_to_all(spread, "wide", 0, 0, tiled=True)
    return got.reshape((n_wide * block.shape[0],) + block.shape[1:])


def scatter_sum(terms, axis_name, parts):
    got = lax.all_to_all(terms.astype(jnp.bfloat16), axis_name, 0, 0, tiled=True)
    got = got.reshape((parts, terms.shape[0] // parts) + terms.shape[1:])
    return jnp.sum(got.astype(jnp.float32), axis=0)


def per_device(patches, vit_gain, vit_qkv, vit_in, vit_attn_out, vit_mlp_out, proj):
    n_wide = lax.axis_size("wide")
    n_narrow = lax.axis_size("narrow")
    w = lax.axis_index("wide")
    n = lax.axis_index("narrow")
    local_rows = patches.shape[0]
    images = patches.shape[1]
    flat_local = local_rows * images
    feature_block = vit_in.shape[0]
    heads_here = vit_qkv.shape[2]
    head_width = vit_qkv.shape[3]
    qkv_cols = 3 * heads_here * head_width
    narrow_start = n * feature_block
    normed = layer_norm(patches, vit_gain)
    normed_part = lax.dynamic_slice_in_dim(normed, narrow_start, feature_block, 2)
    in_weight = jnp.concatenate([vit_qkv.reshape(feature_block, qkv_cols), vit_in], axis=1)
    flat_rows = gather_wide(normed_part.reshape(flat_local, feature_block), n_wide)
    joined = jnp.dot(flat_rows, in_weight, preferred_element_type=jnp.float32)
    row_count = n_wide * local_rows
    partial_in = joined.reshape(row_count, images, -1)
    summed_in = lax.psum(partial_in.astype(jnp.bfloat16), "narrow").astype(jnp.float32)
    qkv_all = (
        summed_in[..., :qkv_cols]
        .astype(jnp.bfloat16)
        .reshape(row_count, images, 3, heads_here, head_width)
    )
    activated = jax.nn.gelu(summed_in[..., qkv_cols:], approximate=False).astype(jnp.bfloat16)
    mixed_heads = attend(qkv_all[:, :, 0], qkv_all[:, :, 1], qkv_all[:, :, 2])
    heads_rows = mixed_heads.reshape(row_count * images, heads_here * head_width)
    units_rows = activated.reshape(row_count * images, -1)
    branch_terms = jnp.dot(heads_rows, vit_attn_out, preferred_element_type=jnp.float32)
    branch_terms = branch_terms + jnp.dot(
        units_rows, vit_mlp_out, preferred_element_type=jnp.float32
    )
    branch_sum = scatter_sum(branch_terms, "wide", n_wide)
    own_columns = lax.dynamic_slice_in_dim(patches, narrow_start, feature_block, 2)
    vit_output = (
        own_columns.reshape(flat_local, feature_block).astype(jnp.float32) + branch_sum
    ).astype(jnp.bfloat16)
    output_rows = gather_wide(vit_output, n_wide)
    partial_encoded = jnp.dot(output_rows, proj, preferred_element_type=jnp.float32)
    encoded_piece = scatter_sum(partial_encoded, "narrow", n_narrow).astype(jnp.bfloat16)
    ratio = n_wide // n_narrow
    enc_block = proj.shape[1]
    pieces = encoded_piece.reshape(ratio, flat_local, enc_block)
    columns = []
    for i in range(ratio):
        got = None
        for j in range(ratio):
            pairs = [
                (src_w * n_narrow + src_n, (ratio * src_n + j) * n_narrow + src_w // ratio)
                for src_w in range(i, n_wide, ratio)
                for src_n in range(n_narrow)
            ]
            moved = lax.ppermute(pieces[j], ("wide", "narrow"), pairs)
            got = moved if got is None else jnp.where(w % ratio == j, moved, got)
        columns.append(got)
    encoded = jnp.concatenate(columns, axis=1)
    return encoded.reshape(local_rows, images, ratio * enc_block)


def solution(mesh):
    return jax.shard_map(
        per_device,
        mesh=mesh,
        in_specs=(
            P("wide", "dp", None),
            P(),
            P("narrow", None, "wide", None),
            P("narrow", "wide"),
            P("wide", "narrow"),
            P("wide", "narrow"),
            P("narrow", "wide"),
        ),
        out_specs=P("wide", "dp", "narrow"),
        check_vma=False,
    )
```

```python
import math

import jax
import jax.numpy as jnp
from jax import lax
from jax.sharding import PartitionSpec as P


def layer_norm(inputs, gain_row):
    widened = inputs.astype(jnp.float32)
    centred = widened - jnp.mean(widened, axis=-1, keepdims=True)
    variance = jnp.mean(centred * centred, axis=-1, keepdims=True)
    return (centred * lax.rsqrt(variance + 1e-06) * gain_row).astype(jnp.bfloat16)


def attend(queries, keys_all, values_all):
    score_scale = 1.0 / math.sqrt(queries.shape[-1])
    scores = (
        jnp.einsum("pihd,qihd->ihpq", queries, keys_all, preferred_element_type=jnp.float32)
        * score_scale
    )
    highest = jnp.max(scores, axis=-1, keepdims=True)
    exponentials = jnp.exp(scores - highest)
    totals = jnp.sum(exponentials, axis=-1)
    weights = exponentials.astype(jnp.bfloat16)
    mixed_sum = jnp.einsum(
        "ihpq,qihd->pihd", weights, values_all, preferred_element_type=jnp.float32
    )
    return (mixed_sum / jnp.transpose(totals, (2, 0, 1))[..., None]).astype(jnp.bfloat16)


def gather_wide(block, n_wide):
    spread = jnp.broadcast_to(block[None], (n_wide,) + block.shape)
    got = lax.all_to_all(spread, "wide", 0, 0, tiled=True)
    return got.reshape((n_wide * block.shape[0],) + block.shape[1:])


def scatter_sum(terms, axis_name, parts):
    got = lax.all_to_all(terms.astype(jnp.bfloat16), axis_name, 0, 0, tiled=True)
    got = got.reshape((parts, terms.shape[0] // parts) + terms.shape[1:])
    return jnp.sum(got.astype(jnp.float32), axis=0)


def per_device(patches, vit_gain, vit_qkv, vit_in, vit_attn_out, vit_mlp_out, proj):
    n_wide = lax.axis_size("wide")
    n_narrow = lax.axis_size("narrow")
    w = lax.axis_index("wide")
    n = lax.axis_index("narrow")
    local_rows = patches.shape[0]
    images = patches.shape[1]
    flat_local = local_rows * images
    feature_block = vit_in.shape[0]
    heads_here = vit_qkv.shape[2]
    head_width = vit_qkv.shape[3]
    narrow_start = n * feature_block
    normed = layer_norm(patches, vit_gain)
    normed_part = lax.dynamic_slice_in_dim(normed, narrow_start, feature_block, 2)
    flat_rows = gather_wide(normed_part.reshape(flat_local, feature_block), n_wide)
    row_count = n_wide * local_rows
    qkv_part = jnp.einsum(
        "rf,fthd->rthd", flat_rows, vit_qkv, preferred_element_type=jnp.float32
    ).astype(jnp.bfloat16)
    hidden_part = jnp.dot(flat_rows, vit_in, preferred_element_type=jnp.float32).astype(
        jnp.bfloat16
    )
    qkv_sum, hidden_sum = lax.psum((qkv_part, hidden_part), "narrow")
    qkv_all = qkv_sum.reshape(row_count, images, 3, heads_here, head_width)
    activated = jax.nn.gelu(hidden_sum.astype(jnp.float32), approximate=False).astype(
        jnp.bfloat16
    )
    mixed_heads = attend(qkv_all[:, :, 0], qkv_all[:, :, 1], qkv_all[:, :, 2])
    heads_rows = mixed_heads.reshape(row_count * images, heads_here * head_width)
    units_rows = activated.reshape(row_count * images, -1)
    branch_terms = jnp.dot(heads_rows, vit_attn_out, preferred_element_type=jnp.float32)
    branch_terms = branch_terms + jnp.dot(
        units_rows, vit_mlp_out, preferred_element_type=jnp.float32
    )
    branch_sum = scatter_sum(branch_terms, "wide", n_wide)
    own_columns = lax.dynamic_slice_in_dim(patches, narrow_start, feature_block, 2)
    vit_output = (
        own_columns.reshape(flat_local, feature_block).astype(jnp.float32) + branch_sum
    ).astype(jnp.bfloat16)
    output_rows = gather_wide(vit_output, n_wide)
    partial_encoded = jnp.dot(output_rows, proj, preferred_element_type=jnp.float32)
    encoded_piece = scatter_sum(partial_encoded, "narrow", n_narrow).astype(jnp.bfloat16)
    ratio = n_wide // n_narrow
    enc_block = proj.shape[1]
    pieces = encoded_piece.reshape(ratio, flat_local, enc_block)
    columns = []
    for i in range(ratio):
        got = None
        for j in range(ratio):
            pairs = [
                (src_w * n_narrow + src_n, (ratio * src_n + j) * n_narrow + src_w // ratio)
                for src_w in range(i, n_wide, ratio)
                for src_n in range(n_narrow)
            ]
            moved = lax.ppermute(pieces[j], ("wide", "narrow"), pairs)
            got = moved if got is None else jnp.where(w % ratio == j, moved, got)
        columns.append(got)
    encoded = jnp.concatenate(columns, axis=1)
    return encoded.reshape(local_rows, images, ratio * enc_block)


def solution(mesh):
    return jax.shard_map(
        per_device,
        mesh=mesh,
        in_specs=(
            P("wide", "dp", None),
            P(),
            P("narrow", None, "wide", None),
            P("narrow", "wide"),
            P("wide", "narrow"),
            P("wide", "narrow"),
            P("narrow", "wide"),
        ),
        out_specs=P("wide", "dp", "narrow"),
        check_vma=False,
    )
```

```python
import math

import jax
import jax.numpy as jnp
from jax import lax
from jax.sharding import PartitionSpec as P


def layer_norm(inputs, gain_row):
    widened = inputs.astype(jnp.float32)
    centred = widened - jnp.mean(widened, axis=-1, keepdims=True)
    variance = jnp.mean(centred * centred, axis=-1, keepdims=True)
    return (centred * lax.rsqrt(variance + 1e-06) * gain_row).astype(jnp.bfloat16)


def attend(queries, keys_all, values_all):
    score_scale = 1.0 / math.sqrt(queries.shape[-1])
    scores = (
        jnp.einsum("pihd,qihd->ihpq", queries, keys_all, preferred_element_type=jnp.float32)
        * score_scale
    )
    highest = jnp.max(scores, axis=-1, keepdims=True)
    exponentials = jnp.exp(scores - highest)
    totals = jnp.sum(exponentials, axis=-1)
    weights = exponentials.astype(jnp.bfloat16)
    mixed_sum = jnp.einsum(
        "ihpq,qihd->pihd", weights, values_all, preferred_element_type=jnp.float32
    )
    return (mixed_sum / jnp.transpose(totals, (2, 0, 1))[..., None]).astype(jnp.bfloat16)


def gather_wide(block, n_wide):
    spread = jnp.broadcast_to(block[None], (n_wide,) + block.shape)
    got = lax.all_to_all(spread, "wide", 0, 0, tiled=True)
    return got.reshape((n_wide * block.shape[0],) + block.shape[1:])


def scatter_sum(terms, axis_name, parts):
    got = lax.all_to_all(terms.astype(jnp.bfloat16), axis_name, 0, 0, tiled=True)
    got = got.reshape((parts, terms.shape[0] // parts) + terms.shape[1:])
    return jnp.sum(got.astype(jnp.float32), axis=0)


def per_device(patches, vit_gain, vit_qkv, vit_in, vit_attn_out, vit_mlp_out, proj):
    n_wide = lax.axis_size("wide")
    n_narrow = lax.axis_size("narrow")
    w = lax.axis_index("wide")
    n = lax.axis_index("narrow")
    local_rows = patches.shape[0]
    images = patches.shape[1]
    flat_local = local_rows * images
    feature_block = vit_in.shape[0]
    heads_here = vit_qkv.shape[2]
    head_width = vit_qkv.shape[3]
    narrow_start = n * feature_block
    normed = layer_norm(patches, vit_gain)
    normed_part = lax.dynamic_slice_in_dim(normed, narrow_start, feature_block, 2)
    flat_rows = gather_wide(normed_part.reshape(flat_local, feature_block), n_wide)
    row_count = n_wide * local_rows
    qkv_part = jnp.einsum(
        "rf,fthd->rthd", flat_rows, vit_qkv, preferred_element_type=jnp.float32
    ).astype(jnp.bfloat16)
    hidden_part = jnp.dot(flat_rows, vit_in, preferred_element_type=jnp.float32).astype(
        jnp.bfloat16
    )
    qkv_part, hidden_part, proj_source = lax.optimization_barrier((qkv_part, hidden_part, proj))
    qkv_sum, hidden_sum = lax.psum((qkv_part, hidden_part), "narrow")
    proj_all = gather_wide(proj_source, n_wide)
    qkv_sum, hidden_sum, proj_all = lax.optimization_barrier((qkv_sum, hidden_sum, proj_all))
    qkv_all = qkv_sum.reshape(row_count, images, 3, heads_here, head_width)
    activated = jax.nn.gelu(hidden_sum.astype(jnp.float32), approximate=False).astype(
        jnp.bfloat16
    )
    mixed_heads = attend(qkv_all[:, :, 0], qkv_all[:, :, 1], qkv_all[:, :, 2])
    heads_rows = mixed_heads.reshape(row_count * images, heads_here * head_width)
    units_rows = activated.reshape(row_count * images, -1)
    branch_terms = jnp.dot(heads_rows, vit_attn_out, preferred_element_type=jnp.float32)
    branch_terms = branch_terms + jnp.dot(
        units_rows, vit_mlp_out, preferred_element_type=jnp.float32
    )
    branch_sum = scatter_sum(branch_terms, "wide", n_wide)
    own_columns = lax.dynamic_slice_in_dim(patches, narrow_start, feature_block, 2)
    vit_output = (
        own_columns.reshape(flat_local, feature_block).astype(jnp.float32) + branch_sum
    ).astype(jnp.bfloat16)
    proj_all = proj_all.reshape(n_wide, feature_block, proj.shape[1])
    partial_encoded = jnp.einsum(
        "rf,wfc->rwc", vit_output, proj_all, preferred_element_type=jnp.float32
    ).astype(jnp.bfloat16)
    partial_encoded = partial_encoded.reshape(flat_local, n_wide * proj.shape[1])
    got = lax.all_to_all(partial_encoded, "narrow", 1, 0, tiled=True)
    got = got.reshape(n_narrow, flat_local, -1)
    encoded = jnp.sum(got.astype(jnp.float32), axis=0).astype(jnp.bfloat16)
    return encoded.reshape(local_rows, images, -1)


def solution(mesh):
    return jax.shard_map(
        per_device,
        mesh=mesh,
        in_specs=(
            P("wide", "dp", None),
            P(),
            P("narrow", None, "wide", None),
            P("narrow", "wide"),
            P("wide", "narrow"),
            P("wide", "narrow"),
            P("narrow", "wide"),
        ),
        out_specs=P("wide", "dp", "narrow"),
        check_vma=False,
    )
```

```python
import math

import jax
import jax.numpy as jnp
from jax import lax
from jax.sharding import PartitionSpec as P


def layer_norm(inputs, gain_row):
    widened = inputs.astype(jnp.float32)
    centred = widened - jnp.mean(widened, axis=-1, keepdims=True)
    variance = jnp.mean(centred * centred, axis=-1, keepdims=True)
    return (centred * lax.rsqrt(variance + 1e-06) * gain_row).astype(jnp.bfloat16)


def attend(queries, keys_all, values_all):
    score_scale = 1.0 / math.sqrt(queries.shape[-1])
    scores = (
        jnp.einsum("pihd,qihd->ihpq", queries, keys_all, preferred_element_type=jnp.float32)
        * score_scale
    )
    highest = jnp.max(scores, axis=-1, keepdims=True)
    exponentials = jnp.exp(scores - highest)
    totals = jnp.sum(exponentials, axis=-1)
    weights = exponentials.astype(jnp.bfloat16)
    mixed_sum = jnp.einsum(
        "ihpq,qihd->pihd", weights, values_all, preferred_element_type=jnp.float32
    )
    return (mixed_sum / jnp.transpose(totals, (2, 0, 1))[..., None]).astype(jnp.bfloat16)


def gather_wide(block, n_wide):
    spread = jnp.broadcast_to(block[None], (n_wide,) + block.shape)
    got = lax.all_to_all(spread, "wide", 0, 0, tiled=True)
    return got.reshape((n_wide * block.shape[0],) + block.shape[1:])


def scatter_sum(terms, axis_name, parts):
    got = lax.all_to_all(terms.astype(jnp.bfloat16), axis_name, 0, 0, tiled=True)
    got = got.reshape((parts, terms.shape[0] // parts) + terms.shape[1:])
    return jnp.sum(got.astype(jnp.float32), axis=0)


def per_device(patches, vit_gain, vit_qkv, vit_in, vit_attn_out, vit_mlp_out, proj):
    n_wide = lax.axis_size("wide")
    n_narrow = lax.axis_size("narrow")
    w = lax.axis_index("wide")
    n = lax.axis_index("narrow")
    local_rows = patches.shape[0]
    images = patches.shape[1]
    flat_local = local_rows * images
    feature_block = vit_in.shape[0]
    heads_here = vit_qkv.shape[2]
    head_width = vit_qkv.shape[3]
    narrow_start = n * feature_block
    normed = layer_norm(patches, vit_gain)
    normed_part = lax.dynamic_slice_in_dim(normed, narrow_start, feature_block, 2)
    flat_rows = gather_wide(normed_part.reshape(flat_local, feature_block), n_wide)
    row_count = n_wide * local_rows
    qkv_part = jnp.einsum(
        "rf,fthd->rthd", flat_rows, vit_qkv, preferred_element_type=jnp.float32
    ).astype(jnp.bfloat16)
    hidden_part = jnp.dot(flat_rows, vit_in, preferred_element_type=jnp.float32).astype(
        jnp.bfloat16
    )
    qkv_part, hidden_part, proj_source = lax.optimization_barrier((qkv_part, hidden_part, proj))
    qkv_sum, hidden_sum = lax.psum((qkv_part, hidden_part), "narrow")
    proj_all = gather_wide(proj_source, n_wide)
    qkv_sum, hidden_sum, proj_all = lax.optimization_barrier((qkv_sum, hidden_sum, proj_all))
    qkv_all = qkv_sum.reshape(row_count, images, 3, heads_here, head_width)
    activated = jax.nn.gelu(hidden_sum.astype(jnp.float32), approximate=False).astype(
        jnp.bfloat16
    )
    activated = lax.optimization_barrier(activated)
    mixed_heads = attend(qkv_all[:, :, 0], qkv_all[:, :, 1], qkv_all[:, :, 2])
    heads_rows = mixed_heads.reshape(row_count * images, heads_here * head_width)
    units_rows = activated.reshape(row_count * images, -1)
    branch_terms = jnp.dot(heads_rows, vit_attn_out, preferred_element_type=jnp.float32)
    branch_terms = branch_terms + jnp.dot(
        units_rows, vit_mlp_out, preferred_element_type=jnp.float32
    )
    branch_sum = scatter_sum(branch_terms, "wide", n_wide)
    own_columns = lax.dynamic_slice_in_dim(patches, narrow_start, feature_block, 2)
    vit_output = (
        own_columns.reshape(flat_local, feature_block).astype(jnp.float32) + branch_sum
    ).astype(jnp.bfloat16)
    proj_all = proj_all.reshape(n_wide, feature_block, proj.shape[1])
    partial_encoded = jnp.einsum(
        "rf,wfc->rwc", vit_output, proj_all, preferred_element_type=jnp.float32
    ).astype(jnp.bfloat16)
    partial_encoded = partial_encoded.reshape(flat_local, n_wide * proj.shape[1])
    got = lax.all_to_all(partial_encoded, "narrow", 1, 0, tiled=True)
    got = got.reshape(n_narrow, flat_local, -1)
    encoded = jnp.sum(got.astype(jnp.float32), axis=0).astype(jnp.bfloat16)
    return encoded.reshape(local_rows, images, -1)


def solution(mesh):
    return jax.shard_map(
        per_device,
        mesh=mesh,
        in_specs=(
            P("wide", "dp", None),
            P(),
            P("narrow", None, "wide", None),
            P("narrow", "wide"),
            P("wide", "narrow"),
            P("wide", "narrow"),
            P("narrow", "wide"),
        ),
        out_specs=P("wide", "dp", "narrow"),
        check_vma=False,
    )
```

```python
import math

import jax
import jax.numpy as jnp
from jax import lax
from jax.sharding import PartitionSpec as P


def layer_norm(inputs, gain_row):
    widened = inputs.astype(jnp.float32)
    centred = widened - jnp.mean(widened, axis=-1, keepdims=True)
    variance = jnp.mean(centred * centred, axis=-1, keepdims=True)
    return (centred * lax.rsqrt(variance + 1e-06) * gain_row).astype(jnp.bfloat16)


def attend(queries, keys_all, values_all):
    score_scale = 1.0 / math.sqrt(queries.shape[-1])
    scores = (
        jnp.einsum("pihd,qihd->ihpq", queries, keys_all, preferred_element_type=jnp.float32)
        * score_scale
    )
    highest = jnp.max(scores, axis=-1, keepdims=True)
    exponentials = jnp.exp(scores - highest)
    totals = jnp.sum(exponentials, axis=-1)
    weights = exponentials.astype(jnp.bfloat16)
    mixed_sum = jnp.einsum(
        "ihpq,qihd->pihd", weights, values_all, preferred_element_type=jnp.float32
    )
    return (mixed_sum / jnp.transpose(totals, (2, 0, 1))[..., None]).astype(jnp.bfloat16)


def gather_wide(block, n_wide):
    spread = jnp.broadcast_to(block[None], (n_wide,) + block.shape)
    got = lax.all_to_all(spread, "wide", 0, 0, tiled=True)
    return got.reshape((n_wide * block.shape[0],) + block.shape[1:])


def scatter_sum(terms, axis_name, parts):
    got = lax.all_to_all(terms.astype(jnp.bfloat16), axis_name, 0, 0, tiled=True)
    got = got.reshape((parts, terms.shape[0] // parts) + terms.shape[1:])
    return jnp.sum(got.astype(jnp.float32), axis=0)


def per_device(patches, vit_gain, vit_qkv, vit_in, vit_attn_out, vit_mlp_out, proj):
    n_wide = lax.axis_size("wide")
    n_narrow = lax.axis_size("narrow")
    w = lax.axis_index("wide")
    n = lax.axis_index("narrow")
    local_rows = patches.shape[0]
    images = patches.shape[1]
    flat_local = local_rows * images
    feature_block = vit_in.shape[0]
    heads_here = vit_qkv.shape[2]
    head_width = vit_qkv.shape[3]
    narrow_start = n * feature_block
    normed = layer_norm(patches, vit_gain)
    normed_part = lax.dynamic_slice_in_dim(normed, narrow_start, feature_block, 2)
    flat_rows = gather_wide(normed_part.reshape(flat_local, feature_block), n_wide)
    row_count = n_wide * local_rows
    qkv_part = jnp.einsum(
        "rf,fthd->rthd", flat_rows, vit_qkv, preferred_element_type=jnp.float32
    ).astype(jnp.bfloat16)
    hidden_part = jnp.dot(flat_rows, vit_in, preferred_element_type=jnp.float32).astype(
        jnp.bfloat16
    )
    qkv_part, hidden_part, proj_source = lax.optimization_barrier((qkv_part, hidden_part, proj))
    qkv_sum, hidden_sum = lax.psum((qkv_part, hidden_part), "narrow")
    proj_all = gather_wide(proj_source, n_wide)
    qkv_sum, hidden_sum, proj_all = lax.optimization_barrier((qkv_sum, hidden_sum, proj_all))
    qkv_all = qkv_sum.reshape(row_count, images, 3, heads_here, head_width)
    activated = jax.nn.gelu(hidden_sum.astype(jnp.float32), approximate=False).astype(
        jnp.bfloat16
    )
    activated = lax.optimization_barrier(activated)
    mixed_heads = attend(qkv_all[:, :, 0], qkv_all[:, :, 1], qkv_all[:, :, 2])
    heads_rows = mixed_heads.reshape(row_count * images, heads_here * head_width)
    units_rows = activated.reshape(row_count * images, -1)
    branch_terms = jnp.dot(heads_rows, vit_attn_out, preferred_element_type=jnp.float32)
    branch_terms = branch_terms + jnp.dot(
        units_rows, vit_mlp_out, preferred_element_type=jnp.float32
    )
    branch_sum = scatter_sum(branch_terms, "wide", n_wide)
    own_columns = lax.dynamic_slice_in_dim(patches, narrow_start, feature_block, 2)
    vit_output = (
        own_columns.reshape(flat_local, feature_block).astype(jnp.float32) + branch_sum
    ).astype(jnp.bfloat16)
    proj_all = proj_all.reshape(n_narrow, n_wide // n_narrow, feature_block, proj.shape[1])
    partial_encoded = jnp.einsum(
        "rf,nkfc->nrkc", vit_output, proj_all, preferred_element_type=jnp.float32
    ).astype(jnp.bfloat16)
    partial_encoded = partial_encoded.reshape(n_narrow, flat_local, -1)
    got = lax.all_to_all(partial_encoded, "narrow", 0, 0, tiled=True)
    encoded = jnp.sum(got.astype(jnp.float32), axis=0).astype(jnp.bfloat16)
    return encoded.reshape(local_rows, images, -1)


def solution(mesh):
    return jax.shard_map(
        per_device,
        mesh=mesh,
        in_specs=(
            P("wide", "dp", None),
            P(),
            P("narrow", None, "wide", None),
            P("narrow", "wide"),
            P("wide", "narrow"),
            P("wide", "narrow"),
            P("narrow", "wide"),
        ),
        out_specs=P("wide", "dp", "narrow"),
        check_vma=False,
    )
```

```python
import math

import jax
import jax.numpy as jnp
from jax import lax
from jax.sharding import PartitionSpec as P


def layer_norm(inputs, gain_row):
    widened = inputs.astype(jnp.float32)
    centred = widened - jnp.mean(widened, axis=-1, keepdims=True)
    variance = jnp.mean(centred * centred, axis=-1, keepdims=True)
    return (centred * lax.rsqrt(variance + 1e-06) * gain_row).astype(jnp.bfloat16)


def attend(queries, keys_all, values_all):
    score_scale = 1.0 / math.sqrt(queries.shape[-1])
    scores = (
        jnp.einsum("pihd,qihd->ihpq", queries, keys_all, preferred_element_type=jnp.float32)
        * score_scale
    )
    highest = jnp.max(scores, axis=-1, keepdims=True)
    exponentials = jnp.exp(scores - highest)
    totals = jnp.sum(exponentials, axis=-1)
    weights = exponentials.astype(jnp.bfloat16)
    mixed_sum = jnp.einsum(
        "ihpq,qihd->pihd", weights, values_all, preferred_element_type=jnp.float32
    )
    return (mixed_sum / jnp.transpose(totals, (2, 0, 1))[..., None]).astype(jnp.bfloat16)


def gather_wide(block, n_wide):
    spread = jnp.broadcast_to(block[None], (n_wide,) + block.shape)
    got = lax.all_to_all(spread, "wide", 0, 0, tiled=True)
    return got.reshape((n_wide * block.shape[0],) + block.shape[1:])


def scatter_sum(terms, axis_name, parts):
    got = lax.all_to_all(terms.astype(jnp.bfloat16), axis_name, 0, 0, tiled=True)
    got = got.reshape((parts, terms.shape[0] // parts) + terms.shape[1:])
    return jnp.sum(got.astype(jnp.float32), axis=0)


def per_device(patches, vit_gain, vit_qkv, vit_in, vit_attn_out, vit_mlp_out, proj):
    n_wide = lax.axis_size("wide")
    n_narrow = lax.axis_size("narrow")
    w = lax.axis_index("wide")
    n = lax.axis_index("narrow")
    local_rows = patches.shape[0]
    images = patches.shape[1]
    flat_local = local_rows * images
    feature_block = vit_in.shape[0]
    heads_here = vit_qkv.shape[2]
    head_width = vit_qkv.shape[3]
    narrow_start = n * feature_block
    normed = layer_norm(patches, vit_gain)
    normed_part = lax.dynamic_slice_in_dim(normed, narrow_start, feature_block, 2)
    flat_rows = gather_wide(normed_part.reshape(flat_local, feature_block), n_wide)
    row_count = n_wide * local_rows
    qkv_part = jnp.einsum(
        "rf,fthd->rthd", flat_rows, vit_qkv, preferred_element_type=jnp.float32
    ).astype(jnp.bfloat16)
    hidden_part = jnp.dot(flat_rows, vit_in, preferred_element_type=jnp.float32).astype(
        jnp.bfloat16
    )
    qkv_part, hidden_part, proj_source = lax.optimization_barrier((qkv_part, hidden_part, proj))
    qkv_sum, hidden_sum = lax.psum((qkv_part, hidden_part), "narrow")
    proj_all = gather_wide(proj_source, n_wide)
    enc_cols = proj.shape[1]
    proj_all = proj_all.reshape(n_narrow, n_wide // n_narrow, feature_block, enc_cols)
    proj_all = jnp.transpose(proj_all, (0, 2, 1, 3)).reshape(n_narrow, feature_block, -1)
    qkv_sum, hidden_sum, proj_all = lax.optimization_barrier((qkv_sum, hidden_sum, proj_all))
    qkv_all = qkv_sum.reshape(row_count, images, 3, heads_here, head_width)
    activated = jax.nn.gelu(hidden_sum.astype(jnp.float32), approximate=False).astype(
        jnp.bfloat16
    )
    activated = lax.optimization_barrier(activated)
    mixed_heads = attend(qkv_all[:, :, 0], qkv_all[:, :, 1], qkv_all[:, :, 2])
    heads_rows = mixed_heads.reshape(row_count * images, heads_here * head_width)
    units_rows = activated.reshape(row_count * images, -1)
    branch_terms = jnp.dot(heads_rows, vit_attn_out, preferred_element_type=jnp.float32)
    branch_terms = branch_terms + jnp.dot(
        units_rows, vit_mlp_out, preferred_element_type=jnp.float32
    )
    branch_sum = scatter_sum(branch_terms, "wide", n_wide)
    own_columns = lax.dynamic_slice_in_dim(patches, narrow_start, feature_block, 2)
    vit_output = (
        own_columns.reshape(flat_local, feature_block).astype(jnp.float32) + branch_sum
    ).astype(jnp.bfloat16)
    partial_encoded = jnp.einsum(
        "rf,nfc->nrc", vit_output, proj_all, preferred_element_type=jnp.float32
    ).astype(jnp.bfloat16)
    got = lax.all_to_all(partial_encoded, "narrow", 0, 0, tiled=True)
    encoded = jnp.sum(got.astype(jnp.float32), axis=0).astype(jnp.bfloat16)
    return encoded.reshape(local_rows, images, -1)


def solution(mesh):
    return jax.shard_map(
        per_device,
        mesh=mesh,
        in_specs=(
            P("wide", "dp", None),
            P(),
            P("narrow", None, "wide", None),
            P("narrow", "wide"),
            P("wide", "narrow"),
            P("wide", "narrow"),
            P("narrow", "wide"),
        ),
        out_specs=P("wide", "dp", "narrow"),
        check_vma=False,
    )
```

```python
import math

import jax
import jax.numpy as jnp
from jax import lax
from jax.sharding import PartitionSpec as P


def layer_norm(inputs, gain_row):
    widened = inputs.astype(jnp.float32)
    centred = widened - jnp.mean(widened, axis=-1, keepdims=True)
    variance = jnp.mean(centred * centred, axis=-1, keepdims=True)
    return (centred * lax.rsqrt(variance + 1e-06) * gain_row).astype(jnp.bfloat16)


def attend(queries, keys_all, values_all):
    score_scale = 1.0 / math.sqrt(queries.shape[-1])
    scores = (
        jnp.einsum("pihd,qihd->ihpq", queries, keys_all, preferred_element_type=jnp.float32)
        * score_scale
    )
    highest = jnp.max(scores, axis=-1, keepdims=True)
    exponentials = jnp.exp(scores - highest)
    totals = jnp.sum(exponentials, axis=-1)
    weights = exponentials.astype(jnp.bfloat16)
    mixed_sum = jnp.einsum(
        "ihpq,qihd->pihd", weights, values_all, preferred_element_type=jnp.float32
    )
    return (mixed_sum / jnp.transpose(totals, (2, 0, 1))[..., None]).astype(jnp.bfloat16)


def gather_wide(block, n_wide):
    spread = jnp.broadcast_to(block[None], (n_wide,) + block.shape)
    got = lax.all_to_all(spread, "wide", 0, 0, tiled=True)
    return got.reshape((n_wide * block.shape[0],) + block.shape[1:])


def scatter_sum(terms, axis_name, parts):
    got = lax.all_to_all(terms.astype(jnp.bfloat16), axis_name, 0, 0, tiled=True)
    got = got.reshape((parts, terms.shape[0] // parts) + terms.shape[1:])
    return jnp.sum(got.astype(jnp.float32), axis=0)


def per_device(patches, vit_gain, vit_qkv, vit_in, vit_attn_out, vit_mlp_out, proj):
    n_wide = lax.axis_size("wide")
    n_narrow = lax.axis_size("narrow")
    w = lax.axis_index("wide")
    n = lax.axis_index("narrow")
    local_rows = patches.shape[0]
    images = patches.shape[1]
    flat_local = local_rows * images
    feature_block = vit_in.shape[0]
    heads_here = vit_qkv.shape[2]
    head_width = vit_qkv.shape[3]
    narrow_start = n * feature_block
    pick = (jnp.arange(n_narrow) == n).astype(jnp.float32)
    gain_part = jnp.sum(vit_gain.reshape(n_narrow, feature_block) * pick[:, None], axis=0)
    widened = patches.astype(jnp.float32)
    centred = widened - jnp.mean(widened, axis=-1, keepdims=True)
    variance = jnp.mean(centred * centred, axis=-1, keepdims=True)
    centred_part = lax.dynamic_slice_in_dim(centred, narrow_start, feature_block, 2)
    normed_part = (centred_part * lax.rsqrt(variance + 1e-06) * gain_part).astype(jnp.bfloat16)
    flat_rows = gather_wide(normed_part.reshape(flat_local, feature_block), n_wide)
    row_count = n_wide * local_rows
    qkv_part = jnp.einsum(
        "rf,fthd->rthd", flat_rows, vit_qkv, preferred_element_type=jnp.float32
    ).astype(jnp.bfloat16)
    hidden_part = jnp.dot(flat_rows, vit_in, preferred_element_type=jnp.float32).astype(
        jnp.bfloat16
    )
    qkv_part, hidden_part, proj_source = lax.optimization_barrier((qkv_part, hidden_part, proj))
    qkv_sum, hidden_sum = lax.psum((qkv_part, hidden_part), "narrow")
    proj_all = gather_wide(proj_source, n_wide)
    qkv_sum, hidden_sum, proj_all = lax.optimization_barrier((qkv_sum, hidden_sum, proj_all))
    qkv_all = qkv_sum.reshape(row_count, images, 3, heads_here, head_width)
    activated = jax.nn.gelu(hidden_sum.astype(jnp.float32), approximate=False).astype(
        jnp.bfloat16
    )
    activated = lax.optimization_barrier(activated)
    mixed_heads = attend(qkv_all[:, :, 0], qkv_all[:, :, 1], qkv_all[:, :, 2])
    heads_rows = mixed_heads.reshape(row_count * images, heads_here * head_width)
    units_rows = activated.reshape(row_count * images, -1)
    branch_terms = jnp.dot(heads_rows, vit_attn_out, preferred_element_type=jnp.float32)
    branch_terms = branch_terms + jnp.dot(
        units_rows, vit_mlp_out, preferred_element_type=jnp.float32
    )
    branch_sum = scatter_sum(branch_terms, "wide", n_wide)
    own_columns = lax.dynamic_slice_in_dim(patches, narrow_start, feature_block, 2)
    vit_output = (
        own_columns.reshape(flat_local, feature_block).astype(jnp.float32) + branch_sum
    ).astype(jnp.bfloat16)
    proj_all = proj_all.reshape(n_narrow, n_wide // n_narrow, feature_block, proj.shape[1])
    partial_encoded = jnp.einsum(
        "rf,nkfc->nrkc", vit_output, proj_all, preferred_element_type=jnp.float32
    ).astype(jnp.bfloat16)
    partial_encoded = partial_encoded.reshape(n_narrow, flat_local, -1)
    got = lax.all_to_all(partial_encoded, "narrow", 0, 0, tiled=True)
    encoded = jnp.sum(got.astype(jnp.float32), axis=0).astype(jnp.bfloat16)
    return encoded.reshape(local_rows, images, -1)


def solution(mesh):
    return jax.shard_map(
        per_device,
        mesh=mesh,
        in_specs=(
            P("wide", "dp", None),
            P(),
            P("narrow", None, "wide", None),
            P("narrow", "wide"),
            P("wide", "narrow"),
            P("wide", "narrow"),
            P("narrow", "wide"),
        ),
        out_specs=P("wide", "dp", "narrow"),
        check_vma=False,
    )
```

```python
import math

import jax
import jax.numpy as jnp
from jax import lax
from jax.sharding import PartitionSpec as P


def layer_norm(inputs, gain_row):
    widened = inputs.astype(jnp.float32)
    centred = widened - jnp.mean(widened, axis=-1, keepdims=True)
    variance = jnp.mean(centred * centred, axis=-1, keepdims=True)
    return (centred * lax.rsqrt(variance + 1e-06) * gain_row).astype(jnp.bfloat16)


def attend(queries, keys_all, values_all):
    score_scale = 1.0 / math.sqrt(queries.shape[-1])
    scores = (
        jnp.einsum("pihd,qihd->ihpq", queries, keys_all, preferred_element_type=jnp.float32)
        * score_scale
    )
    highest = jnp.max(scores, axis=-1, keepdims=True)
    exponentials = jnp.exp(scores - highest)
    totals = jnp.sum(exponentials, axis=-1)
    weights = exponentials.astype(jnp.bfloat16)
    mixed_sum = jnp.einsum(
        "ihpq,qihd->pihd", weights, values_all, preferred_element_type=jnp.float32
    )
    return (mixed_sum / jnp.transpose(totals, (2, 0, 1))[..., None]).astype(jnp.bfloat16)


def gather_wide(block, n_wide):
    spread = jnp.broadcast_to(block[None], (n_wide,) + block.shape)
    got = lax.all_to_all(spread, "wide", 0, 0, tiled=True)
    return got.reshape((n_wide * block.shape[0],) + block.shape[1:])


def scatter_sum(terms, axis_name, parts):
    got = lax.all_to_all(terms.astype(jnp.bfloat16), axis_name, 0, 0, tiled=True)
    got = got.reshape((parts, terms.shape[0] // parts) + terms.shape[1:])
    return jnp.sum(got.astype(jnp.float32), axis=0)


def per_device(patches, vit_gain, vit_qkv, vit_in, vit_attn_out, vit_mlp_out, proj):
    n_wide = lax.axis_size("wide")
    n_narrow = lax.axis_size("narrow")
    w = lax.axis_index("wide")
    n = lax.axis_index("narrow")
    local_rows = patches.shape[0]
    images = patches.shape[1]
    flat_local = local_rows * images
    feature_block = vit_in.shape[0]
    heads_here = vit_qkv.shape[2]
    head_width = vit_qkv.shape[3]
    narrow_start = n * feature_block
    pick = (jnp.arange(n_narrow) == n).astype(jnp.float32)
    gain_part = jnp.sum(vit_gain.reshape(n_narrow, feature_block) * pick[:, None], axis=0)
    widened = patches.astype(jnp.float32)
    row_mean = jnp.mean(widened, axis=-1, keepdims=True)
    centred = widened - row_mean
    variance = jnp.mean(centred * centred, axis=-1, keepdims=True)
    widened_part = lax.dynamic_slice_in_dim(patches, narrow_start, feature_block, 2)
    centred_part = widened_part.astype(jnp.float32) - row_mean
    normed_part = (centred_part * lax.rsqrt(variance + 1e-06) * gain_part).astype(jnp.bfloat16)
    flat_rows = gather_wide(normed_part.reshape(flat_local, feature_block), n_wide)
    row_count = n_wide * local_rows
    qkv_part = jnp.einsum(
        "rf,fthd->rthd", flat_rows, vit_qkv, preferred_element_type=jnp.float32
    ).astype(jnp.bfloat16)
    hidden_part = jnp.dot(flat_rows, vit_in, preferred_element_type=jnp.float32).astype(
        jnp.bfloat16
    )
    qkv_part, hidden_part, proj_source = lax.optimization_barrier((qkv_part, hidden_part, proj))
    qkv_sum, hidden_sum = lax.psum((qkv_part, hidden_part), "narrow")
    proj_all = gather_wide(proj_source, n_wide)
    qkv_sum, hidden_sum, proj_all = lax.optimization_barrier((qkv_sum, hidden_sum, proj_all))
    qkv_all = qkv_sum.reshape(row_count, images, 3, heads_here, head_width)
    activated = jax.nn.gelu(hidden_sum.astype(jnp.float32), approximate=False).astype(
        jnp.bfloat16
    )
    activated = lax.optimization_barrier(activated)
    mixed_heads = attend(qkv_all[:, :, 0], qkv_all[:, :, 1], qkv_all[:, :, 2])
    heads_rows = mixed_heads.reshape(row_count * images, heads_here * head_width)
    units_rows = activated.reshape(row_count * images, -1)
    branch_terms = jnp.dot(heads_rows, vit_attn_out, preferred_element_type=jnp.float32)
    branch_terms = branch_terms + jnp.dot(
        units_rows, vit_mlp_out, preferred_element_type=jnp.float32
    )
    branch_sum = scatter_sum(branch_terms, "wide", n_wide)
    own_columns = lax.dynamic_slice_in_dim(patches, narrow_start, feature_block, 2)
    vit_output = (
        own_columns.reshape(flat_local, feature_block).astype(jnp.float32) + branch_sum
    ).astype(jnp.bfloat16)
    proj_all = proj_all.reshape(n_narrow, n_wide // n_narrow, feature_block, proj.shape[1])
    partial_encoded = jnp.einsum(
        "rf,nkfc->nrkc", vit_output, proj_all, preferred_element_type=jnp.float32
    ).astype(jnp.bfloat16)
    partial_encoded = partial_encoded.reshape(n_narrow, flat_local, -1)
    got = lax.all_to_all(partial_encoded, "narrow", 0, 0, tiled=True)
    encoded = jnp.sum(got.astype(jnp.float32), axis=0).astype(jnp.bfloat16)
    return encoded.reshape(local_rows, images, -1)


def solution(mesh):
    return jax.shard_map(
        per_device,
        mesh=mesh,
        in_specs=(
            P("wide", "dp", None),
            P(),
            P("narrow", None, "wide", None),
            P("narrow", "wide"),
            P("wide", "narrow"),
            P("wide", "narrow"),
            P("narrow", "wide"),
        ),
        out_specs=P("wide", "dp", "narrow"),
        check_vma=False,
    )
```
